128 devices in a mesh: wide: 64 (over x, z, y), narrow: 2 (over core).
Axes of the slice: x: 4, y: 4, z: 4, core: 2. Of those that a mesh axis runs over, the one named last changes fastest.
Arguments:
- features: bfloat16 [16384, 512], P(('wide', 'narrow')), may hold values from -6 to 6
- weight: bfloat16 [512, 512], replicated, may hold values from -0.25 to 0.25
- tile_cols: int32 [128, 2, 48], P('wide', 'narrow'), may hold values from 0 to 63
- tile_count: int32 [128, 2], P('wide', 'narrow'), may hold values from 6 to 48, as said below
- tile_weights: bfloat16 [128, 2, 48, 128, 128], P('wide', 'narrow'), may hold values from 0 to 1, as said below
- cotangent: bfloat16 [16384, 512], P(('wide', 'narrow')), may hold values from -6 to 6
Outputs:
- activated: bfloat16 [16384, 512], P(('wide', 'narrow'))
- grad_features: bfloat16 [16384, 512], P(('wide', 'narrow'))
- grad_weight: float32 [512, 512], replicated
The draws below stay inside these ranges and needn't reach their ends.
Inputs may be any that keep to these rules, and one draw needn't show every extreme that they name: `tile_count`: live slots of one tile row and residue; the largest equals 48 in every draw. `tile_weights`: edge weights; most entries of a tile are zero.
All inputs are finite; a program needn't handle non-finite values.
Results may differ from the reference program's by a relative error of at most 0.007.
Values may be sent and summed in bfloat16 or wider, within the bound.
No kernel may reach another device: no remote copies, remote signals or barrier semaphores. Data moves between devices by JAX's collectives and lax.ppermute only.
A program may use at most 128 MiB of HBM per device.

```python
import math
import jax
import jax.numpy as jnp
import numpy as np
from jax import lax

F = 512
TILE = 128
TMAX = 48
NODES = 16384
TROWS = 128
N_WIDE = 64
N_NARROW = 2


def draw_tile_count(key, part):
    first, second = jax.random.split(key)
    counts = jax.random.randint(first, (TROWS, N_NARROW), TMAX // 8, TMAX + 1)
    place = jax.random.randint(second, (), 0, TROWS * N_NARROW)
    flat = counts.reshape(-1)
    flat = jnp.where(jnp.arange(TROWS * N_NARROW) == place, TMAX, flat)
    return flat.reshape(TROWS, N_NARROW).astype(jnp.int32)


def draw_tile_weights(key, part):
    share_key = jax.random.fold_in(key, 11)
    pick_key = jax.random.fold_in(key, 12)
    value_key = jax.random.fold_in(key, 13)
    share = jax.random.randint(share_key, (TROWS, N_NARROW, TMAX, 1, 1), 2, 13)
    picks = jax.random.randint(pick_key, (TROWS, N_NARROW, TMAX, TILE, TILE), 0, 100)
    keep = (picks < share).astype(jnp.float32)
    values = jax.random.uniform(value_key, (TROWS, N_NARROW, TMAX, TILE, TILE), jnp.float32, 0.0, 1.0)
    return (values * keep).astype(jnp.bfloat16)


def set_ends(array, key, low, high):
    spot = [jax.random.randint(jax.random.fold_in(key, axis), (), 0, length) for axis, length in enumerate(array.shape)]
    longest = array.shape.index(max(array.shape))
    next_to = spot[:longest] + [(spot[longest] + 1) % array.shape[longest]] + spot[longest + 1:]
    return array.at[tuple(spot)].set(low).at[tuple(next_to)].set(high)


def shard_levels(rng, shape, cuts, least, largest):
    def one(axis_at, parts):
        draws = jax.random.uniform(jax.random.fold_in(jax.random.fold_in(rng, 6), axis_at), (parts,), jnp.float32, least / len(cuts), largest / len(cuts))
        return jnp.repeat(jnp.exp(draws), shape[axis_at] // parts).reshape((-1,) + (1,) * (len(shape) - axis_at - 1))

    gain = one(*cuts[0])
    for cut in cuts[1:]:
        gain = gain * one(*cut)
    return gain


def cumulative_ranks(count, slope):
    loads = [(1 << 20) // math.isqrt(rank ** slope) + 1 for rank in range(1, count + 1)]
    spread = 1 + sum(loads) // (1 << 30)
    return np.cumsum(np.array([max(1, weight // spread) for weight in loads]))


def ranked(key, extent, number_of, lean):
    grid = cumulative_ranks(number_of, lean)
    lot = jax.random.randint(jax.random.fold_in(key, 1), extent, 0, int(grid[number_of - 1]))
    grade = jnp.searchsorted(jnp.asarray(grid, jnp.int32), lot, side="right")
    return jax.random.permutation(jax.random.fold_in(key, 2), number_of)[grade].astype(jnp.int32)


def noise(own_key, shape, width, most, shards=(), kind=jnp.bfloat16):
    factor_of = shard_levels(own_key, shape, shards, -0.22, 0.18) if shards else 1.0
    array = jax.random.normal(own_key, shape, jnp.float32) * width * factor_of
    return jnp.minimum(jnp.maximum(array, -most), most).astype(kind)


def setup_inputs(seed: int = 0) -> dict:
    key_list = jax.random.split(jax.random.key(seed), 7)
    return {
        "features": noise(key_list[0], (NODES, F), 1.0, 6.0, ((0, 128),)),
        "weight": noise(key_list[1], (F, F), F ** -0.5, 0.25),
        "tile_cols": set_ends(ranked(key_list[2], (TROWS, N_NARROW, TMAX), N_WIDE, 2), jax.random.fold_in(key_list[2], 3), 0, N_WIDE - 1).astype(jnp.int32),
        "tile_count": draw_tile_count(jax.random.fold_in(key_list[6], 71), 0),
        "tile_weights": draw_tile_weights(jax.random.fold_in(key_list[6], 71), 0),
        "cotangent": noise(key_list[5], (NODES, F), 1.0, 6.0, ((0, 128),)),
    }


def row_panel(cols, count, weights):
    tiles = weights.astype(jnp.float32)
    live = (jnp.arange(TMAX, dtype=jnp.int32)[None, :] < count[:, None]).astype(jnp.float32)
    onehot = (cols[..., None] == jnp.arange(N_WIDE, dtype=jnp.int32)).astype(jnp.float32) * live[..., None]
    return jnp.einsum('skj,sktc->sjtc', onehot, tiles)

def rounded(panel):
    return lax.optimization_barrier(panel.astype(jnp.bfloat16)).astype(jnp.float32)

def reference(features, weight, tile_cols, tile_count, tile_weights, cotangent):
    projected = jnp.dot(features, weight, preferred_element_type=jnp.float32).astype(jnp.bfloat16)
    blocks = projected.astype(jnp.float32).reshape(N_WIDE, N_NARROW, TILE, F)

    def forward_row(index):
        panel = row_panel(tile_cols[index], tile_count[index], tile_weights[index])
        degree = 1.0 + lax.optimization_barrier(jnp.sum(panel, axis=(0, 1, 3)))
        aggregate = jnp.einsum('sjtc,jscf->tf', rounded(panel), blocks)
        return (aggregate, degree)
    aggregate, degree = lax.map(forward_row, jnp.arange(TROWS, dtype=jnp.int32))
    aggregate = aggregate.reshape(NODES, F)
    scale = lax.rsqrt(degree.reshape(NODES))[:, None]
    preact = (aggregate + projected.astype(jnp.float32)) * scale
    activated = jax.nn.silu(preact).astype(jnp.bfloat16)
    sig = jax.nn.sigmoid(preact)
    upstream = (cotangent.astype(jnp.float32) * sig * (1.0 + preact * (1.0 - sig)) * scale).astype(jnp.bfloat16)
    up_blocks = upstream.astype(jnp.float32).reshape(TROWS, TILE, F)

    def backward_row(total, index):
        panel = rounded(row_panel(tile_cols[index], tile_count[index], tile_weights[index]))
        return (total + jnp.einsum('sjtc,tf->jscf', panel, up_blocks[index]), None)
    start = jnp.zeros((N_WIDE, N_NARROW, TILE, F), jnp.float32)
    total, unused = lax.scan(backward_row, start, jnp.arange(TROWS, dtype=jnp.int32))
    message = (total.reshape(NODES, F) + upstream.astype(jnp.float32)).astype(jnp.bfloat16)
    grad_features = jnp.dot(message, weight.T, preferred_element_type=jnp.float32).astype(jnp.bfloat16)
    grad_weight = jnp.dot(features.T, message, preferred_element_type=jnp.float32)
    return (activated, grad_features, grad_weight)
```

```python
import jax
import jax.numpy as jnp
from jax import lax
from jax.sharding import PartitionSpec as P


def per_device(features, weight, tile_cols, tile_count, tile_weights, cotangent):
    tile = features.shape[0]
    width = features.shape[1]
    copies = tile_cols.shape[0]
    slots = tile_cols.shape[2]
    owners = lax.axis_size("wide")
    columns = tile_cols[:, 0, :]
    counts = tile_count[:, 0]
    tiles = tile_weights[:, 0]
    live = (jnp.arange(slots, dtype=jnp.int32)[None, :] < counts[:, None]).astype(jnp.bfloat16)
    onehot = (columns[..., None] == jnp.arange(owners, dtype=jnp.int32)).astype(
        jnp.bfloat16
    ) * live[..., None]
    dense = jnp.einsum("skj,sktc->stjc", onehot, tiles, preferred_element_type=jnp.float32).reshape(
        copies * tile, owners * tile
    )
    degree = 1.0 + lax.psum(jnp.sum(dense, axis=1), "narrow")
    scale = lax.rsqrt(degree)
    panel = dense.astype(jnp.bfloat16)
    projected = jnp.dot(features, weight, preferred_element_type=jnp.float32).astype(jnp.bfloat16)
    own = lax.axis_index("narrow")
    part_cols = panel
    partial_sum = jnp.dot(
        part_cols,
        lax.all_gather(projected, "wide", axis=0, tiled=True),
        preferred_element_type=jnp.float32,
    )
    selector = (jnp.arange(copies, dtype=jnp.int32) == own).astype(jnp.float32)
    self_term = selector[:, None, None] * projected.astype(jnp.float32)[None]
    partial_sum = partial_sum + self_term.reshape(copies * tile, width)
    own_scale = lax.dynamic_slice_in_dim(scale, own * tile, tile, 0)[:, None]
    preact = lax.psum_scatter(partial_sum, "narrow", scatter_dimension=0, tiled=True) * own_scale
    activated = jax.nn.silu(preact).astype(jnp.bfloat16)
    sig = jax.nn.sigmoid(preact)
    own_grad = (
        cotangent.astype(jnp.float32) * sig * (1.0 + preact * (1.0 - sig)) * own_scale
    ).astype(jnp.bfloat16)
    all_grad = lax.all_gather(own_grad, "narrow", axis=0, tiled=True)
    part_cols = panel
    terms = lax.dot_general(
        part_cols, all_grad, (((0,), (0,)), ((), ())), preferred_element_type=jnp.float32
    )
    sent = lax.all_to_all(
        terms.astype(jnp.bfloat16).reshape(owners, tile, width), "wide", 0, 0, tiled=True
    )
    gathered_sum = jnp.sum(sent.astype(jnp.float32), axis=0)
    message = (gathered_sum + own_grad.astype(jnp.float32)).astype(jnp.bfloat16)
    grad_features = lax.dot_general(
        message, weight, (((1,), (1,)), ((), ())), preferred_element_type=jnp.float32
    ).astype(jnp.bfloat16)
    weight_terms = lax.dot_general(
        features, message, (((0,), (0,)), ((), ())), preferred_element_type=jnp.float32
    )
    devices = owners * lax.axis_size("narrow")
    rows = width // devices
    mine = lax.all_to_all(
        weight_terms.reshape(devices, rows, width), ("wide", "narrow"), 0, 0, tiled=True
    )
    mine = jnp.sum(mine, axis=0)
    grad_weight = lax.all_to_all(
        jnp.broadcast_to(mine[None], (devices, rows, width)), ("wide", "narrow"), 0, 0, tiled=True
    ).reshape(width, width)
    return (activated, grad_features, grad_weight)


def solution(mesh):
    return jax.shard_map(
        per_device,
        mesh=mesh,
        in_specs=(
            P(("wide", "narrow"), None),
            P(),
            P("wide", "narrow", None),
            P("wide", "narrow"),
            P("wide", "narrow", None, None, None),
            P(("wide", "narrow"), None),
        ),
        out_specs=(P(("wide", "narrow"), None), P(("wide", "narrow"), None), P()),
        check_vma=False,
    )
```

```python
import jax
import jax.numpy as jnp
from jax import lax
from jax.sharding import PartitionSpec as P

CHUNKS = 4


def per_device(features, weight, tile_cols, tile_count, tile_weights, cotangent):
    tile = features.shape[0]
    width = features.shape[1]
    copies = tile_cols.shape[0]
    slots = tile_cols.shape[2]
    owners = lax.axis_size("wide")
    columns = tile_cols[:, 0, :]
    counts = tile_count[:, 0]
    tiles = tile_weights[:, 0]
    live = (jnp.arange(slots, dtype=jnp.int32)[None, :] < counts[:, None]).astype(jnp.bfloat16)
    onehot = (columns[..., None] == jnp.arange(owners, dtype=jnp.int32)).astype(
        jnp.bfloat16
    ) * live[..., None]
    dense = jnp.einsum("skj,sktc->stjc", onehot, tiles, preferred_element_type=jnp.float32).reshape(
        copies * tile, owners * tile
    )
    degree = 1.0 + lax.psum(jnp.sum(dense, axis=1), "narrow")
    scale = lax.rsqrt(degree)
    panel = dense.astype(jnp.bfloat16)
    projected = jnp.dot(features, weight, preferred_element_type=jnp.float32).astype(jnp.bfloat16)
    own = lax.axis_index("narrow")
    selector = (jnp.arange(copies, dtype=jnp.int32) == own).astype(jnp.float32)
    own_scale = lax.dynamic_slice_in_dim(scale, own * tile, tile, 0)[:, None]
    step = width // CHUNKS
    activated_parts = []
    message_parts = []
    for j in range(CHUNKS):
        part = projected[:, j * step:(j + 1) * step]
        gathered = lax.all_gather(part, "wide", axis=0, tiled=True)
        if j > 0:
            gathered, _ = lax.optimization_barrier((gathered, last_sent))
        partial_sum = jnp.dot(panel, gathered, preferred_element_type=jnp.float32)
        self_term = selector[:, None, None] * part.astype(jnp.float32)[None]
        partial_sum = partial_sum + self_term.reshape(copies * tile, step)
        halves = lax.all_to_all(
            partial_sum.reshape(copies, tile, step), "narrow", 0, 0, tiled=True
        )
        preact = jnp.sum(halves, axis=0) * own_scale
        activated_parts.append(jax.nn.silu(preact).astype(jnp.bfloat16))
        sig = jax.nn.sigmoid(preact)
        cot = cotangent[:, j * step:(j + 1) * step].astype(jnp.float32)
        own_grad = (cot * sig * (1.0 + preact * (1.0 - sig)) * own_scale).astype(jnp.bfloat16)
        all_grad = lax.all_gather(own_grad, "narrow", axis=0, tiled=True)
        terms = lax.dot_general(
            panel, all_grad, (((0,), (0,)), ((), ())), preferred_element_type=jnp.float32
        )
        last_terms = terms.astype(jnp.bfloat16)
        sent = lax.all_to_all(last_terms.reshape(owners, tile, step), "wide", 0, 0, tiled=True)
        last_sent = sent
        gathered_sum = jnp.sum(sent.astype(jnp.float32), axis=0)
        message_parts.append((gathered_sum + own_grad.astype(jnp.float32)).astype(jnp.bfloat16))
    activated = jnp.concatenate(activated_parts, axis=1)
    message = jnp.concatenate(message_parts, axis=1)
    grad_features = lax.dot_general(
        message, weight, (((1,), (1,)), ((), ())), preferred_element_type=jnp.float32
    ).astype(jnp.bfloat16)
    weight_terms = lax.dot_general(
        features, message, (((0,), (0,)), ((), ())), preferred_element_type=jnp.float32
    )
    devices = owners * lax.axis_size("narrow")
    rows = width // devices
    mine = lax.all_to_all(
        weight_terms.reshape(devices, rows, width), ("wide", "narrow"), 0, 0, tiled=True
    )
    mine = jnp.sum(mine, axis=0)
    grad_weight = lax.all_to_all(
        jnp.broadcast_to(mine[None], (devices, rows, width)), ("wide", "narrow"), 0, 0, tiled=True
    ).reshape(width, width)
    return (activated, grad_features, grad_weight)


def solution(mesh):
    return jax.shard_map(
        per_device,
        mesh=mesh,
        in_specs=(
            P(("wide", "narrow"), None),
            P(),
            P("wide", "narrow", None),
            P("wide", "narrow"),
            P("wide", "narrow", None, None, None),
            P(("wide", "narrow"), None),
        ),
        out_specs=(P(("wide", "narrow"), None), P(("wide", "narrow"), None), P()),
        check_vma=False,
    )
```

```python
import jax
import jax.numpy as jnp
from jax import lax
from jax.sharding import PartitionSpec as P


def per_device(features, weight, tile_cols, tile_count, tile_weights, cotangent):
    tile = features.shape[0]
    width = features.shape[1]
    copies = tile_cols.shape[0]
    slots = tile_cols.shape[2]
    owners = lax.axis_size("wide")
    columns = tile_cols[:, 0, :]
    counts = tile_count[:, 0]
    tiles = tile_weights[:, 0]
    gathered_features = lax.all_gather(features, "wide", axis=0, tiled=True)
    live = (jnp.arange(slots, dtype=jnp.int32)[None, :] < counts[:, None]).astype(jnp.bfloat16)
    onehot = (columns[..., None] == jnp.arange(owners, dtype=jnp.int32)).astype(
        jnp.bfloat16
    ) * live[..., None]
    dense = jnp.einsum("skj,sktc->stjc", onehot, tiles, preferred_element_type=jnp.float32).reshape(
        copies * tile, owners * tile
    )
    degree = 1.0 + lax.psum(jnp.sum(dense, axis=1), "narrow")
    scale = lax.rsqrt(degree)
    panel = dense.astype(jnp.bfloat16)
    projected = jnp.dot(features, weight, preferred_element_type=jnp.float32).astype(jnp.bfloat16)
    gathered = jnp.dot(gathered_features, weight, preferred_element_type=jnp.float32).astype(
        jnp.bfloat16
    )
    own = lax.axis_index("narrow")
    partial_sum = jnp.dot(panel, gathered, preferred_element_type=jnp.float32)
    selector = (jnp.arange(copies, dtype=jnp.int32) == own).astype(jnp.float32)
    self_term = selector[:, None, None] * projected.astype(jnp.float32)[None]
    partial_sum = partial_sum + self_term.reshape(copies * tile, width)
    own_scale = lax.dynamic_slice_in_dim(scale, own * tile, tile, 0)[:, None]
    halves = lax.all_to_all(partial_sum.reshape(copies, tile, width), "narrow", 0, 0, tiled=True)
    preact = jnp.sum(halves, axis=0) * own_scale
    activated = jax.nn.silu(preact).astype(jnp.bfloat16)
    sig = jax.nn.sigmoid(preact)
    own_grad = (
        cotangent.astype(jnp.float32) * sig * (1.0 + preact * (1.0 - sig)) * own_scale
    ).astype(jnp.bfloat16)
    all_grad = lax.all_gather(own_grad, "narrow", axis=0, tiled=True)
    terms = lax.dot_general(
        panel, all_grad, (((0,), (0,)), ((), ())), preferred_element_type=jnp.float32
    ).astype(jnp.bfloat16)
    weight_terms = lax.dot_general(
        gathered_features, terms, (((0,), (0,)), ((), ())), preferred_element_type=jnp.float32
    ) + lax.dot_general(
        features, own_grad, (((0,), (0,)), ((), ())), preferred_element_type=jnp.float32
    )
    rows = width // owners
    high = weight_terms.astype(jnp.bfloat16)
    low = (weight_terms - high.astype(jnp.float32)).astype(jnp.bfloat16)
    payload = jnp.concatenate(
        [
            terms.reshape(owners, tile, width),
            high.reshape(owners, rows, width),
            low.reshape(owners, rows, width),
        ],
        axis=1,
    )
    received = lax.all_to_all(payload, "wide", 0, 0, tiled=True)
    band = jnp.sum(
        received[:, tile:tile + rows].astype(jnp.float32)
        + received[:, tile + rows:].astype(jnp.float32),
        axis=0,
    )
    band = lax.psum(band, "narrow")
    grad_weight = lax.all_to_all(
        jnp.broadcast_to(band[None], (owners, rows, width)), "wide", 0, 0, tiled=True
    ).reshape(width, width)
    gathered_sum = jnp.sum(received[:, :tile].astype(jnp.float32), axis=0)
    message = (gathered_sum + own_grad.astype(jnp.float32)).astype(jnp.bfloat16)
    grad_features = lax.dot_general(
        message, weight, (((1,), (1,)), ((), ())), preferred_element_type=jnp.float32
    ).astype(jnp.bfloat16)
    return (activated, grad_features, grad_weight)


def solution(mesh):
    return jax.shard_map(
        per_device,
        mesh=mesh,
        in_specs=(
            P(("wide", "narrow"), None),
            P(),
            P("wide", "narrow", None),
            P("wide", "narrow"),
            P("wide", "narrow", None, None, None),
            P(("wide", "narrow"), None),
        ),
        out_specs=(P(("wide", "narrow"), None), P(("wide", "narrow"), None), P()),
        check_vma=False,
    )
```

```python
import jax
import jax.numpy as jnp
from jax import lax
from jax.sharding import PartitionSpec as P


def per_device(features, weight, tile_cols, tile_count, tile_weights, cotangent):
    tile = features.shape[0]
    width = features.shape[1]
    copies = tile_cols.shape[0]
    slots = tile_cols.shape[2]
    owners = lax.axis_size("wide")
    columns = tile_cols[:, 0, :]
    counts = tile_count[:, 0]
    tiles = tile_weights[:, 0]
    gathered_features = lax.all_gather(features, "wide", axis=0, tiled=True)
    live = (jnp.arange(slots, dtype=jnp.int32)[None, :] < counts[:, None]).astype(jnp.bfloat16)
    onehot = (columns[..., None] == jnp.arange(owners, dtype=jnp.int32)).astype(
        jnp.bfloat16
    ) * live[..., None]
    dense = jnp.einsum("skj,sktc->stjc", onehot, tiles, preferred_element_type=jnp.float32).reshape(
        copies * tile, owners * tile
    )
    degree = 1.0 + lax.psum(jnp.sum(dense, axis=1), "narrow")
    scale = lax.rsqrt(degree)
    panel = dense.astype(jnp.bfloat16)
    projected = jnp.dot(features, weight, preferred_element_type=jnp.float32).astype(jnp.bfloat16)
    own = lax.axis_index("narrow")
    aggregated = jnp.dot(panel, gathered_features, preferred_element_type=jnp.float32)
    partial_sum = jnp.dot(
        aggregated, weight.astype(jnp.float32), precision=lax.Precision.HIGHEST,
        preferred_element_type=jnp.float32,
    )
    selector = (jnp.arange(copies, dtype=jnp.int32) == own).astype(jnp.float32)
    self_term = selector[:, None, None] * projected.astype(jnp.float32)[None]
    partial_sum = partial_sum + self_term.reshape(copies * tile, width)
    own_scale = lax.dynamic_slice_in_dim(scale, own * tile, tile, 0)[:, None]
    halves = lax.all_to_all(partial_sum.reshape(copies, tile, width), "narrow", 0, 0, tiled=True)
    preact = jnp.sum(halves, axis=0) * own_scale
    activated = jax.nn.silu(preact).astype(jnp.bfloat16)
    sig = jax.nn.sigmoid(preact)
    own_grad = (
        cotangent.astype(jnp.float32) * sig * (1.0 + preact * (1.0 - sig)) * own_scale
    ).astype(jnp.bfloat16)
    all_grad = lax.all_gather(own_grad, "narrow", axis=0, tiled=True)
    terms = lax.dot_general(
        panel, all_grad, (((0,), (0,)), ((), ())), preferred_element_type=jnp.float32
    ).astype(jnp.bfloat16)
    weight_terms = lax.dot_general(
        aggregated, all_grad.astype(jnp.float32), (((0,), (0,)), ((), ())),
        precision=lax.Precision.HIGHEST, preferred_element_type=jnp.float32,
    ) + lax.dot_general(
        features, own_grad, (((0,), (0,)), ((), ())), preferred_element_type=jnp.float32
    )
    rows = width // owners
    high = weight_terms.astype(jnp.bfloat16)
    low = (weight_terms - high.astype(jnp.float32)).astype(jnp.bfloat16)
    payload = jnp.concatenate(
        [
            terms.reshape(owners, tile, width),
            high.reshape(owners, rows, width),
            low.reshape(owners, rows, width),
        ],
        axis=1,
    )
    received = lax.all_to_all(payload, "wide", 0, 0, tiled=True)
    band = jnp.sum(
        received[:, tile:tile + rows].astype(jnp.float32)
        + received[:, tile + rows:].astype(jnp.float32),
        axis=0,
    )
    band = lax.psum(band, "narrow")
    grad_weight = lax.all_to_all(
        jnp.broadcast_to(band[None], (owners, rows, width)), "wide", 0, 0, tiled=True
    ).reshape(width, width)
    gathered_sum = jnp.sum(received[:, :tile].astype(jnp.float32), axis=0)
    message = (gathered_sum + own_grad.astype(jnp.float32)).astype(jnp.bfloat16)
    grad_features = lax.dot_general(
        message, weight, (((1,), (1,)), ((), ())), preferred_element_type=jnp.float32
    ).astype(jnp.bfloat16)
    return (activated, grad_features, grad_weight)


def solution(mesh):
    return jax.shard_map(
        per_device,
        mesh=mesh,
        in_specs=(
            P(("wide", "narrow"), None),
            P(),
            P("wide", "narrow", None),
            P("wide", "narrow"),
            P("wide", "narrow", None, None, None),
            P(("wide", "narrow"), None),
        ),
        out_specs=(P(("wide", "narrow"), None), P(("wide", "narrow"), None), P()),
        check_vma=False,
    )
```

```python
import jax
import jax.numpy as jnp
from jax import lax
from jax.sharding import PartitionSpec as P


def per_device(features, weight, tile_cols, tile_count, tile_weights, cotangent):
    tile = features.shape[0]
    width = features.shape[1]
    copies = tile_cols.shape[0]
    slots = tile_cols.shape[2]
    owners = lax.axis_size("wide")
    columns = tile_cols[:, 0, :]
    counts = tile_count[:, 0]
    tiles = tile_weights[:, 0]
    gathered_features = lax.all_gather(features, "wide", axis=0, tiled=True)
    live = (jnp.arange(slots, dtype=jnp.int32)[None, :] < counts[:, None]).astype(jnp.bfloat16)
    onehot = (columns[..., None] == jnp.arange(owners, dtype=jnp.int32)).astype(
        jnp.bfloat16
    ) * live[..., None]
    dense = jnp.einsum("skj,sktc->stjc", onehot, tiles, preferred_element_type=jnp.float32).reshape(
        copies * tile, owners * tile
    )
    degree = 1.0 + lax.psum(jnp.sum(dense, axis=1), "narrow")
    scale = lax.rsqrt(degree)
    panel = dense.astype(jnp.bfloat16)
    projected = jnp.dot(features, weight, preferred_element_type=jnp.float32).astype(jnp.bfloat16)
    own = lax.axis_index("narrow")
    aggregated = jnp.dot(panel, gathered_features, preferred_element_type=jnp.float32)
    partial_sum = jnp.dot(
        aggregated, weight.astype(jnp.float32), precision=lax.Precision.HIGHEST,
        preferred_element_type=jnp.float32,
    )
    selector = (jnp.arange(copies, dtype=jnp.int32) == own).astype(jnp.float32)
    self_term = selector[:, None, None] * projected.astype(jnp.float32)[None]
    partial_sum = partial_sum + self_term.reshape(copies * tile, width)
    own_scale = lax.dynamic_slice_in_dim(scale, own * tile, tile, 0)[:, None]
    halves = lax.all_to_all(partial_sum.reshape(copies, tile, width), "narrow", 0, 0, tiled=True)
    preact = jnp.sum(halves, axis=0) * own_scale
    activated = jax.nn.silu(preact).astype(jnp.bfloat16)
    sig = jax.nn.sigmoid(preact)
    own_grad = (
        cotangent.astype(jnp.float32) * sig * (1.0 + preact * (1.0 - sig)) * own_scale
    ).astype(jnp.bfloat16)
    all_grad = lax.all_gather(own_grad, "narrow", axis=0, tiled=True)
    terms = lax.dot_general(
        panel, all_grad, (((0,), (0,)), ((), ())), preferred_element_type=jnp.float32
    ).astype(jnp.bfloat16)
    weight_terms = lax.dot_general(
        aggregated, all_grad.astype(jnp.float32), (((0,), (0,)), ((), ())),
        precision=lax.Precision.HIGHEST, preferred_element_type=jnp.float32,
    ) + lax.dot_general(
        features, own_grad, (((0,), (0,)), ((), ())), preferred_element_type=jnp.float32
    )
    grad_weight = lax.psum(weight_terms, ("wide", "narrow"))
    received = lax.all_to_all(terms.reshape(owners, tile, width), "wide", 0, 0, tiled=True)
    gathered_sum = jnp.sum(received.astype(jnp.float32), axis=0)
    message = (gathered_sum + own_grad.astype(jnp.float32)).astype(jnp.bfloat16)
    grad_features = lax.dot_general(
        message, weight, (((1,), (1,)), ((), ())), preferred_element_type=jnp.float32
    ).astype(jnp.bfloat16)
    return (activated, grad_features, grad_weight)


def solution(mesh):
    return jax.shard_map(
        per_device,
        mesh=mesh,
        in_specs=(
            P(("wide", "narrow"), None),
            P(),
            P("wide", "narrow", None),
            P("wide", "narrow"),
            P("wide", "narrow", None, None, None),
            P(("wide", "narrow"), None),
        ),
        out_specs=(P(("wide", "narrow"), None), P(("wide", "narrow"), None), P()),
        check_vma=False,
    )
```

```python
import jax
import jax.numpy as jnp
from jax import lax
from jax.sharding import PartitionSpec as P


def per_device(features, weight, tile_cols, tile_count, tile_weights, cotangent):
    tile = features.shape[0]
    width = features.shape[1]
    copies = tile_cols.shape[0]
    slots = tile_cols.shape[2]
    owners = lax.axis_size("wide")
    columns = tile_cols[:, 0, :]
    counts = tile_count[:, 0]
    tiles = tile_weights[:, 0]
    gathered_features = lax.all_gather(features, "wide", axis=0, tiled=True)
    live = (jnp.arange(slots, dtype=jnp.int32)[None, :] < counts[:, None]).astype(jnp.bfloat16)
    onehot = (columns[..., None] == jnp.arange(owners, dtype=jnp.int32)).astype(
        jnp.bfloat16
    ) * live[..., None]
    dense = jnp.einsum("skj,sktc->stjc", onehot, tiles, preferred_element_type=jnp.float32).reshape(
        copies * tile, owners * tile
    )
    degree = 1.0 + lax.psum(jnp.sum(dense, axis=1), "narrow")
    scale = lax.rsqrt(degree)
    panel = dense.astype(jnp.bfloat16)
    panel_t = jnp.einsum(
        "skj,sktc->jcst", onehot, tiles, preferred_element_type=jnp.float32
    ).reshape(owners * tile, copies * tile).astype(jnp.bfloat16)
    projected = jnp.dot(features, weight, preferred_element_type=jnp.float32).astype(jnp.bfloat16)
    own = lax.axis_index("narrow")
    aggregated = jnp.dot(panel, gathered_features, preferred_element_type=jnp.float32)
    partial_sum = jnp.dot(
        aggregated, weight.astype(jnp.float32), precision=lax.Precision.HIGHEST,
        preferred_element_type=jnp.float32,
    )
    selector = (jnp.arange(copies, dtype=jnp.int32) == own).astype(jnp.float32)
    self_term = selector[:, None, None] * projected.astype(jnp.float32)[None]
    partial_sum = partial_sum + self_term.reshape(copies * tile, width)
    own_scale = lax.dynamic_slice_in_dim(scale, own * tile, tile, 0)[:, None]
    halves = lax.all_to_all(partial_sum.reshape(copies, tile, width), "narrow", 0, 0, tiled=True)
    preact = jnp.sum(halves, axis=0) * own_scale
    activated = jax.nn.silu(preact).astype(jnp.bfloat16)
    sig = jax.nn.sigmoid(preact)
    own_grad = (
        cotangent.astype(jnp.float32) * sig * (1.0 + preact * (1.0 - sig)) * own_scale
    ).astype(jnp.bfloat16)
    all_grad = lax.all_gather(own_grad, "narrow", axis=0, tiled=True)
    terms = jnp.dot(panel_t, all_grad, preferred_element_type=jnp.float32).astype(jnp.bfloat16)
    weight_terms = lax.dot_general(
        aggregated, all_grad.astype(jnp.float32), (((0,), (0,)), ((), ())),
        precision=lax.Precision.HIGHEST, preferred_element_type=jnp.float32,
    ) + lax.dot_general(
        features, own_grad, (((0,), (0,)), ((), ())), preferred_element_type=jnp.float32
    )
    rows = width // owners
    high = weight_terms.astype(jnp.bfloat16)
    low = (weight_terms - high.astype(jnp.float32)).astype(jnp.bfloat16)
    payload = jnp.concatenate(
        [
            terms.reshape(owners, tile, width),
            high.reshape(owners, rows, width),
            low.reshape(owners, rows, width),
        ],
        axis=1,
    )
    received = lax.all_to_all(payload, "wide", 0, 0, tiled=True)
    band = jnp.sum(
        received[:, tile:tile + rows].astype(jnp.float32)
        + received[:, tile + rows:].astype(jnp.float32),
        axis=0,
    )
    band = lax.psum(band, "narrow")
    grad_weight = lax.all_to_all(
        jnp.broadcast_to(band[None], (owners, rows, width)), "wide", 0, 0, tiled=True
    ).reshape(width, width)
    gathered_sum = jnp.sum(received[:, :tile].astype(jnp.float32), axis=0)
    message = (gathered_sum + own_grad.astype(jnp.float32)).astype(jnp.bfloat16)
    grad_features = lax.dot_general(
        message, weight, (((1,), (1,)), ((), ())), preferred_element_type=jnp.float32
    ).astype(jnp.bfloat16)
    return (activated, grad_features, grad_weight)


def solution(mesh):
    return jax.shard_map(
        per_device,
        mesh=mesh,
        in_specs=(
            P(("wide", "narrow"), None),
            P(),
            P("wide", "narrow", None),
            P("wide", "narrow"),
            P("wide", "narrow", None, None, None),
            P(("wide", "narrow"), None),
        ),
        out_specs=(P(("wide", "narrow"), None), P(("wide", "narrow"), None), P()),
        check_vma=False,
    )
```

```python
import jax
import jax.numpy as jnp
from jax import lax
from jax.sharding import PartitionSpec as P


def per_device(features, weight, tile_cols, tile_count, tile_weights, cotangent):
    tile = features.shape[0]
    width = features.shape[1]
    copies = tile_cols.shape[0]
    slots = tile_cols.shape[2]
    owners = lax.axis_size("wide")
    columns = tile_cols[:, 0, :]
    counts = tile_count[:, 0]
    tiles = tile_weights[:, 0]
    gathered_features = lax.all_gather(features, "wide", axis=0, tiled=True)
    live = (jnp.arange(slots, dtype=jnp.int32)[None, :] < counts[:, None]).astype(jnp.bfloat16)
    onehot = (columns[..., None] == jnp.arange(owners, dtype=jnp.int32)).astype(
        jnp.bfloat16
    ) * live[..., None]
    dense = jnp.einsum("skj,sktc->stjc", onehot, tiles, preferred_element_type=jnp.float32).reshape(
        copies * tile, owners * tile
    )
    degree = 1.0 + lax.psum(jnp.sum(dense, axis=1), "narrow")
    scale = lax.rsqrt(degree)
    panel = dense.astype(jnp.bfloat16)
    panel_t = jnp.einsum(
        "skj,sktc->jcst", onehot, tiles, preferred_element_type=jnp.float32
    ).reshape(owners * tile, copies * tile).astype(jnp.bfloat16)
    projected = jnp.dot(features, weight, preferred_element_type=jnp.float32).astype(jnp.bfloat16)
    own = lax.axis_index("narrow")
    aggregated = jnp.dot(panel, gathered_features, preferred_element_type=jnp.float32)
    partial_sum = jnp.dot(
        aggregated, weight.astype(jnp.float32), precision=lax.Precision.HIGHEST,
        preferred_element_type=jnp.float32,
    )
    selector = (jnp.arange(copies, dtype=jnp.int32) == own).astype(jnp.float32)
    self_term = selector[:, None, None] * projected.astype(jnp.float32)[None]
    partial_sum = partial_sum + self_term.reshape(copies * tile, width)
    own_scale = lax.dynamic_slice_in_dim(scale, own * tile, tile, 0)[:, None]
    halves = lax.all_to_all(partial_sum.reshape(copies, tile, width), "narrow", 0, 0, tiled=True)
    preact = jnp.sum(halves, axis=0) * own_scale
    activated = jax.nn.silu(preact).astype(jnp.bfloat16)
    sig = jax.nn.sigmoid(preact)
    own_grad = (
        cotangent.astype(jnp.float32) * sig * (1.0 + preact * (1.0 - sig)) * own_scale
    ).astype(jnp.bfloat16)
    all_grad = lax.all_gather(own_grad, "narrow", axis=0, tiled=True)
    terms = jnp.dot(panel_t, all_grad, preferred_element_type=jnp.float32).astype(jnp.bfloat16)
    weight_terms = lax.dot_general(
        aggregated, all_grad.astype(jnp.float32), (((0,), (0,)), ((), ())),
        precision=lax.Precision.HIGHEST, preferred_element_type=jnp.float32,
    ) + lax.dot_general(
        features, own_grad, (((0,), (0,)), ((), ())), preferred_element_type=jnp.float32
    )
    rows = width // owners
    high = weight_terms.astype(jnp.bfloat16)
    low = (weight_terms - high.astype(jnp.float32)).astype(jnp.bfloat16)
    shares = jnp.concatenate(
        [high.reshape(owners, rows, width), low.reshape(owners, rows, width)], axis=1
    )
    shares = lax.all_to_all(shares, "wide", 0, 0, tiled=True)
    band = jnp.sum(
        shares[:, :rows].astype(jnp.float32) + shares[:, rows:].astype(jnp.float32), axis=0
    )
    band = lax.psum(band, "narrow")
    grad_weight = lax.all_to_all(
        jnp.broadcast_to(band[None], (owners, rows, width)), "wide", 0, 0, tiled=True
    ).reshape(width, width)
    received = lax.all_to_all(terms.reshape(owners, tile, width), "wide", 0, 0, tiled=True)
    gathered_sum = jnp.sum(received.astype(jnp.float32), axis=0)
    message = (gathered_sum + own_grad.astype(jnp.float32)).astype(jnp.bfloat16)
    grad_features = lax.dot_general(
        message, weight, (((1,), (1,)), ((), ())), preferred_element_type=jnp.float32
    ).astype(jnp.bfloat16)
    return (activated, grad_features, grad_weight)


def solution(mesh):
    return jax.shard_map(
        per_device,
        mesh=mesh,
        in_specs=(
            P(("wide", "narrow"), None),
            P(),
            P("wide", "narrow", None),
            P("wide", "narrow"),
            P("wide", "narrow", None, None, None),
            P(("wide", "narrow"), None),
        ),
        out_specs=(P(("wide", "narrow"), None), P(("wide", "narrow"), None), P()),
        check_vma=False,
    )
```

```python
import jax
import jax.numpy as jnp
from jax import lax
from jax.sharding import PartitionSpec as P


def per_device(features, weight, tile_cols, tile_count, tile_weights, cotangent):
    tile = features.shape[0]
    width = features.shape[1]
    copies = tile_cols.shape[0]
    slots = tile_cols.shape[2]
    owners = lax.axis_size("wide")
    columns = tile_cols[:, 0, :]
    counts = tile_count[:, 0]
    tiles = tile_weights[:, 0]
    gathered_features = lax.all_gather(features, "wide", axis=0, tiled=True)
    live = (jnp.arange(slots, dtype=jnp.int32)[None, :] < counts[:, None]).astype(jnp.bfloat16)
    onehot = (columns[..., None] == jnp.arange(owners, dtype=jnp.int32)).astype(
        jnp.bfloat16
    ) * live[..., None]
    dense = jnp.einsum("skj,sktc->stjc", onehot, tiles, preferred_element_type=jnp.float32).reshape(
        copies * tile, owners * tile
    )
    degree = 1.0 + lax.psum(jnp.sum(dense, axis=1), "narrow")
    scale = lax.rsqrt(degree)
    panel = dense.astype(jnp.bfloat16)
    projected = jnp.dot(features, weight, preferred_element_type=jnp.float32).astype(jnp.bfloat16)
    own = lax.axis_index("narrow")
    aggregated = jnp.dot(panel, gathered_features, preferred_element_type=jnp.float32)
    partial_sum = jnp.dot(
        aggregated, weight.astype(jnp.float32), precision=lax.Precision.HIGHEST,
        preferred_element_type=jnp.float32,
    )
    selector = (jnp.arange(copies, dtype=jnp.int32) == own).astype(jnp.float32)
    self_term = selector[:, None, None] * projected.astype(jnp.float32)[None]
    partial_sum = partial_sum + self_term.reshape(copies * tile, width)
    pair = lax.axis_size("narrow")
    total = jnp.sum(
        lax.all_to_all(
            jnp.broadcast_to(partial_sum[None], (pair,) + partial_sum.shape), "narrow", 0, 0,
            tiled=True,
        ),
        axis=0,
    )
    preact_both = total * scale[:, None]
    sig = jax.nn.sigmoid(preact_both)
    cot_both = lax.all_gather(cotangent, "narrow", axis=0, tiled=True).astype(jnp.float32)
    all_grad = (
        cot_both * sig * (1.0 + preact_both * (1.0 - sig)) * scale[:, None]
    ).astype(jnp.bfloat16)
    preact = lax.dynamic_slice_in_dim(preact_both, own * tile, tile, 0)
    activated = jax.nn.silu(preact).astype(jnp.bfloat16)
    own_grad = lax.dynamic_slice_in_dim(all_grad, own * tile, tile, 0)
    terms = lax.dot_general(
        panel, all_grad, (((0,), (0,)), ((), ())), preferred_element_type=jnp.float32
    ).astype(jnp.bfloat16)
    weight_terms = lax.dot_general(
        aggregated, all_grad.astype(jnp.float32), (((0,), (0,)), ((), ())),
        precision=lax.Precision.HIGHEST, preferred_element_type=jnp.float32,
    ) + lax.dot_general(
        features, own_grad, (((0,), (0,)), ((), ())), preferred_element_type=jnp.float32
    )
    rows = width // owners
    high = weight_terms.astype(jnp.bfloat16)
    low = (weight_terms - high.astype(jnp.float32)).astype(jnp.bfloat16)
    payload = jnp.concatenate(
        [
            terms.reshape(owners, tile, width),
            high.reshape(owners, rows, width),
            low.reshape(owners, rows, width),
        ],
        axis=1,
    )
    received = lax.all_to_all(payload, "wide", 0, 0, tiled=True)
    band = jnp.sum(
        received[:, tile:tile + rows].astype(jnp.float32)
        + received[:, tile + rows:].astype(jnp.float32),
        axis=0,
    )
    band = lax.psum(band, "narrow")
    grad_weight = lax.all_to_all(
        jnp.broadcast_to(band[None], (owners, rows, width)), "wide", 0, 0, tiled=True
    ).reshape(width, width)
    gathered_sum = jnp.sum(received[:, :tile].astype(jnp.float32), axis=0)
    message = (gathered_sum + own_grad.astype(jnp.float32)).astype(jnp.bfloat16)
    grad_features = lax.dot_general(
        message, weight, (((1,), (1,)), ((), ())), preferred_element_type=jnp.float32
    ).astype(jnp.bfloat16)
    return (activated, grad_features, grad_weight)


def solution(mesh):
    return jax.shard_map(
        per_device,
        mesh=mesh,
        in_specs=(
            P(("wide", "narrow"), None),
            P(),
            P("wide", "narrow", None),
            P("wide", "narrow"),
            P("wide", "narrow", None, None, None),
            P(("wide", "narrow"), None),
        ),
        out_specs=(P(("wide", "narrow"), None), P(("wide", "narrow"), None), P()),
        check_vma=False,
    )
```

```python
import jax
import jax.numpy as jnp
from jax import lax
from jax.sharding import PartitionSpec as P


def per_device(features, weight, tile_cols, tile_count, tile_weights, cotangent):
    tile = features.shape[0]
    width = features.shape[1]
    copies = tile_cols.shape[0]
    slots = tile_cols.shape[2]
    owners = lax.axis_size("wide")
    columns = tile_cols[:, 0, :]
    counts = tile_count[:, 0]
    tiles = tile_weights[:, 0]
    gathered_features = lax.all_gather(features, "wide", axis=0, tiled=True)
    live = (jnp.arange(slots, dtype=jnp.int32)[None, :] < counts[:, None]).astype(jnp.bfloat16)
    onehot = (columns[..., None] == jnp.arange(owners, dtype=jnp.int32)).astype(
        jnp.bfloat16
    ) * live[..., None]
    dense = jnp.einsum("skj,sktc->stjc", onehot, tiles, preferred_element_type=jnp.float32).reshape(
        copies * tile, owners * tile
    )
    degree = 1.0 + lax.psum(jnp.sum(dense, axis=1), "narrow")
    scale = lax.rsqrt(degree)
    panel = dense.astype(jnp.bfloat16)
    projected = jnp.dot(features, weight, preferred_element_type=jnp.float32).astype(jnp.bfloat16)
    own = lax.axis_index("narrow")
    pair = lax.axis_size("narrow")
    aggregated = jnp.dot(panel, gathered_features, preferred_element_type=jnp.float32)
    partial_sum = jnp.dot(
        aggregated, weight.astype(jnp.float32), precision=lax.Precision.HIGHEST,
        preferred_element_type=jnp.float32,
    )
    selector = (jnp.arange(copies, dtype=jnp.int32) == own).astype(jnp.float32)
    self_term = selector[:, None, None] * projected.astype(jnp.float32)[None]
    partial_sum = partial_sum + self_term.reshape(copies * tile, width)
    total = jnp.sum(
        lax.all_to_all(
            jnp.broadcast_to(partial_sum[None], (pair,) + partial_sum.shape), "narrow", 0, 0,
            tiled=True,
        ),
        axis=0,
    )
    preact_both = total * scale[:, None]
    sig = jax.nn.sigmoid(preact_both)
    cot_both = lax.all_gather(cotangent, "narrow", axis=0, tiled=True).astype(jnp.float32)
    all_grad = (
        cot_both * sig * (1.0 + preact_both * (1.0 - sig)) * scale[:, None]
    ).astype(jnp.bfloat16)
    preact = lax.dynamic_slice_in_dim(preact_both, own * tile, tile, 0)
    activated = jax.nn.silu(preact).astype(jnp.bfloat16)
    own_grad = lax.dynamic_slice_in_dim(all_grad, own * tile, tile, 0)
    terms = lax.dot_general(
        panel, all_grad, (((0,), (0,)), ((), ())), preferred_element_type=jnp.float32
    ).astype(jnp.bfloat16)
    weight_terms = lax.dot_general(
        aggregated, all_grad.astype(jnp.float32), (((0,), (0,)), ((), ())),
        precision=lax.Precision.HIGHEST, preferred_element_type=jnp.float32,
    ) + lax.dot_general(
        features, own_grad, (((0,), (0,)), ((), ())), preferred_element_type=jnp.float32
    )
    pair = lax.axis_size("narrow")
    rows = width // (owners * pair)
    shares = lax.all_to_all(
        weight_terms.reshape(owners, pair, rows, width), "narrow", 1, 1, tiled=True
    )
    shares = jnp.sum(shares, axis=1)
    high = shares.astype(jnp.bfloat16)
    low = (shares - high.astype(jnp.float32)).astype(jnp.bfloat16)
    payload = jnp.concatenate([terms.reshape(owners, tile, width), high, low], axis=1)
    received = lax.all_to_all(payload, "wide", 0, 0, tiled=True)
    band = jnp.sum(
        received[:, tile:tile + rows].astype(jnp.float32)
        + received[:, tile + rows:].astype(jnp.float32),
        axis=0,
    )
    grad_weight = lax.all_to_all(
        jnp.broadcast_to(band[None], (owners * pair, rows, width)), ("wide", "narrow"), 0, 0,
        tiled=True,
    ).reshape(width, width)
    gathered_sum = jnp.sum(received[:, :tile].astype(jnp.float32), axis=0)
    message = (gathered_sum + own_grad.astype(jnp.float32)).astype(jnp.bfloat16)
    grad_features = lax.dot_general(
        message, weight, (((1,), (1,)), ((), ())), preferred_element_type=jnp.float32
    ).astype(jnp.bfloat16)
    return (activated, grad_features, grad_weight)


def solution(mesh):
    return jax.shard_map(
        per_device,
        mesh=mesh,
        in_specs=(
            P(("wide", "narrow"), None),
            P(),
            P("wide", "narrow", None),
            P("wide", "narrow"),
            P("wide", "narrow", None, None, None),
            P(("wide", "narrow"), None),
        ),
        out_specs=(P(("wide", "narrow"), None), P(("wide", "narrow"), None), P()),
        check_vma=False,
    )
```

```python
import jax
import jax.numpy as jnp
from jax import lax
from jax.sharding import PartitionSpec as P


def per_device(features, weight, tile_cols, tile_count, tile_weights, cotangent):
    tile = features.shape[0]
    width = features.shape[1]
    copies = tile_cols.shape[0]
    slots = tile_cols.shape[2]
    owners = lax.axis_size("wide")
    columns = tile_cols[:, 0, :]
    counts = tile_count[:, 0]
    tiles = tile_weights[:, 0]
    gathered_features = lax.all_gather(features, "wide", axis=0, tiled=True)
    live = (jnp.arange(slots, dtype=jnp.int32)[None, :] < counts[:, None]).astype(jnp.bfloat16)
    onehot = (columns[..., None] == jnp.arange(owners, dtype=jnp.int32)).astype(
        jnp.bfloat16
    ) * live[..., None]
    dense = jnp.einsum("skj,sktc->stjc", onehot, tiles, preferred_element_type=jnp.float32).reshape(
        copies * tile, owners * tile
    )
    degree = 1.0 + lax.psum(jnp.sum(dense, axis=1), "narrow")
    scale = lax.rsqrt(degree)
    panel = dense.astype(jnp.bfloat16)
    projected = jnp.dot(features, weight, preferred_element_type=jnp.float32).astype(jnp.bfloat16)
    own = lax.axis_index("narrow")
    aggregated = jnp.dot(panel, gathered_features, preferred_element_type=jnp.float32)
    partial_sum = jnp.dot(
        aggregated, weight.astype(jnp.float32), precision=lax.Precision.HIGHEST,
        preferred_element_type=jnp.float32,
    )
    selector = (jnp.arange(copies, dtype=jnp.int32) == own).astype(jnp.float32)
    self_term = selector[:, None, None] * projected.astype(jnp.float32)[None]
    partial_sum = partial_sum + self_term.reshape(copies * tile, width)
    own_scale = lax.dynamic_slice_in_dim(scale, own * tile, tile, 0)[:, None]
    pair = lax.axis_size("narrow")
    mine = lax.dynamic_slice_in_dim(partial_sum, own * tile, tile, 0)
    theirs = lax.dynamic_slice_in_dim(partial_sum, (pair - 1 - own) * tile, tile, 0)
    theirs = lax.ppermute(theirs, "narrow", [(i, pair - 1 - i) for i in range(pair)])
    preact = (mine + theirs) * own_scale
    activated = jax.nn.silu(preact).astype(jnp.bfloat16)
    sig = jax.nn.sigmoid(preact)
    own_grad = (
        cotangent.astype(jnp.float32) * sig * (1.0 + preact * (1.0 - sig)) * own_scale
    ).astype(jnp.bfloat16)
    all_grad = lax.all_gather(own_grad, "narrow", axis=0, tiled=True)
    terms = lax.dot_general(
        panel, all_grad, (((0,), (0,)), ((), ())), preferred_element_type=jnp.float32
    ).astype(jnp.bfloat16)
    weight_terms = lax.dot_general(
        aggregated, all_grad.astype(jnp.float32), (((0,), (0,)), ((), ())),
        precision=lax.Precision.HIGHEST, preferred_element_type=jnp.float32,
    ) + lax.dot_general(
        features, own_grad, (((0,), (0,)), ((), ())), preferred_element_type=jnp.float32
    )
    rows = width // owners
    high = weight_terms.astype(jnp.bfloat16)
    low = (weight_terms - high.astype(jnp.float32)).astype(jnp.bfloat16)
    payload = jnp.concatenate(
        [
            terms.reshape(owners, tile, width),
            high.reshape(owners, rows, width),
            low.reshape(owners, rows, width),
        ],
        axis=1,
    )
    received = lax.all_to_all(payload, "wide", 0, 0, tiled=True)
    band = jnp.sum(
        received[:, tile:tile + rows].astype(jnp.float32)
        + received[:, tile + rows:].astype(jnp.float32),
        axis=0,
    )
    band = lax.psum(band, "narrow")
    grad_weight = lax.all_to_all(
        jnp.broadcast_to(band[None], (owners, rows, width)), "wide", 0, 0, tiled=True
    ).reshape(width, width)
    gathered_sum = jnp.sum(received[:, :tile].astype(jnp.float32), axis=0)
    message = (gathered_sum + own_grad.astype(jnp.float32)).astype(jnp.bfloat16)
    grad_features = lax.dot_general(
        message, weight, (((1,), (1,)), ((), ())), preferred_element_type=jnp.float32
    ).astype(jnp.bfloat16)
    return (activated, grad_features, grad_weight)


def solution(mesh):
    return jax.shard_map(
        per_device,
        mesh=mesh,
        in_specs=(
            P(("wide", "narrow"), None),
            P(),
            P("wide", "narrow", None),
            P("wide", "narrow"),
            P("wide", "narrow", None, None, None),
            P(("wide", "narrow"), None),
        ),
        out_specs=(P(("wide", "narrow"), None), P(("wide", "narrow"), None), P()),
        check_vma=False,
    )
```

```python
import jax
import jax.numpy as jnp
from jax import lax
from jax.sharding import PartitionSpec as P


def per_device(features, weight, tile_cols, tile_count, tile_weights, cotangent):
    tile = features.shape[0]
    width = features.shape[1]
    copies = tile_cols.shape[0]
    slots = tile_cols.shape[2]
    owners = lax.axis_size("wide")
    columns = tile_cols[:, 0, :]
    counts = tile_count[:, 0]
    tiles = tile_weights[:, 0]
    gathered_features = lax.all_gather(features, "wide", axis=0, tiled=True)
    live = (jnp.arange(slots, dtype=jnp.int32)[None, :] < counts[:, None]).astype(jnp.bfloat16)
    onehot = (columns[..., None] == jnp.arange(owners, dtype=jnp.int32)).astype(
        jnp.bfloat16
    ) * live[..., None]
    dense = jnp.einsum("skj,sktc->stjc", onehot, tiles, preferred_element_type=jnp.float32).reshape(
        copies * tile, owners * tile
    )
    degree = 1.0 + lax.psum(jnp.sum(dense, axis=1), "narrow")
    scale = lax.rsqrt(degree)
    panel = dense.astype(jnp.bfloat16)
    projected = jnp.dot(features, weight, preferred_element_type=jnp.float32).astype(jnp.bfloat16)
    own = lax.axis_index("narrow")
    aggregated = jnp.dot(panel, gathered_features, preferred_element_type=jnp.float32)
    partial_sum = jnp.dot(
        aggregated, weight.astype(jnp.float32), precision=lax.Precision.HIGHEST,
        preferred_element_type=jnp.float32,
    )
    selector = (jnp.arange(copies, dtype=jnp.int32) == own).astype(jnp.float32)
    self_term = selector[:, None, None] * projected.astype(jnp.float32)[None]
    partial_sum = partial_sum + self_term.reshape(copies * tile, width)
    own_scale = lax.dynamic_slice_in_dim(scale, own * tile, tile, 0)[:, None]
    halves = lax.all_to_all(partial_sum.reshape(copies, tile, width), "narrow", 0, 0, tiled=True)
    preact = jnp.sum(halves, axis=0) * own_scale
    activated = jax.nn.silu(preact).astype(jnp.bfloat16)
    sig = jax.nn.sigmoid(preact)
    own_grad = (
        cotangent.astype(jnp.float32) * sig * (1.0 + preact * (1.0 - sig)) * own_scale
    ).astype(jnp.bfloat16)
    all_grad = lax.all_gather(own_grad, "narrow", axis=0, tiled=True)
    terms = lax.dot_general(
        panel, all_grad, (((0,), (0,)), ((), ())), preferred_element_type=jnp.float32
    ).astype(jnp.bfloat16)
    weight_terms = lax.dot_general(
        aggregated, all_grad.astype(jnp.float32), (((0,), (0,)), ((), ())),
        precision=lax.Precision.HIGHEST, preferred_element_type=jnp.float32,
    ) + lax.dot_general(
        features, own_grad, (((0,), (0,)), ((), ())), preferred_element_type=jnp.float32
    )
    rows = width // owners
    payload = jnp.concatenate(
        [terms.reshape(owners, tile, width), weight_terms.astype(jnp.bfloat16).reshape(owners, rows, width)],
        axis=1,
    )
    received = lax.all_to_all(payload, "wide", 0, 0, tiled=True)
    band = jnp.sum(received[:, tile:].astype(jnp.float32), axis=0)
    band = lax.psum(band, "narrow").astype(jnp.bfloat16)
    grad_weight = lax.all_to_all(
        jnp.broadcast_to(band[None], (owners, rows, width)), "wide", 0, 0, tiled=True
    ).reshape(width, width).astype(jnp.float32)
    gathered_sum = jnp.sum(received[:, :tile].astype(jnp.float32), axis=0)
    message = (gathered_sum + own_grad.astype(jnp.float32)).astype(jnp.bfloat16)
    grad_features = lax.dot_general(
        message, weight, (((1,), (1,)), ((), ())), preferred_element_type=jnp.float32
    ).astype(jnp.bfloat16)
    return (activated, grad_features, grad_weight)


def solution(mesh):
    return jax.shard_map(
        per_device,
        mesh=mesh,
        in_specs=(
            P(("wide", "narrow"), None),
            P(),
            P("wide", "narrow", None),
            P("wide", "narrow"),
            P("wide", "narrow", None, None, None),
            P(("wide", "narrow"), None),
        ),
        out_specs=(P(("wide", "narrow"), None), P(("wide", "narrow"), None), P()),
        check_vma=False,
    )
```

```python
import jax
import jax.numpy as jnp
from jax import lax
from jax.sharding import PartitionSpec as P


def per_device(features, weight, tile_cols, tile_count, tile_weights, cotangent):
    tile = features.shape[0]
    width = features.shape[1]
    copies = tile_cols.shape[0]
    slots = tile_cols.shape[2]
    owners = lax.axis_size("wide")
    columns = tile_cols[:, 0, :]
    counts = tile_count[:, 0]
    tiles = tile_weights[:, 0]
    gathered_features = lax.all_gather(features, "wide", axis=0, tiled=True)
    live = (jnp.arange(slots, dtype=jnp.int32)[None, :] < counts[:, None]).astype(jnp.bfloat16)
    onehot = (columns[..., None] == jnp.arange(owners, dtype=jnp.int32)).astype(
        jnp.bfloat16
    ) * live[..., None]
    dense = jnp.einsum("skj,sktc->stjc", onehot, tiles, preferred_element_type=jnp.float32).reshape(
        copies * tile, owners * tile
    )
    degree = 1.0 + lax.psum(jnp.sum(dense, axis=1), "narrow")
    scale = lax.rsqrt(degree)
    panel = dense.astype(jnp.bfloat16)
    projected = jnp.dot(features, weight, preferred_element_type=jnp.float32).astype(jnp.bfloat16)
    own = lax.axis_index("narrow")
    aggregated = jnp.dot(panel, gathered_features, preferred_element_type=jnp.float32)
    partial_sum = jnp.dot(
        aggregated, weight.astype(jnp.float32), precision=lax.Precision.HIGHEST,
        preferred_element_type=jnp.float32,
    )
    selector = (jnp.arange(copies, dtype=jnp.int32) == own).astype(jnp.float32)
    self_term = selector[:, None, None] * projected.astype(jnp.float32)[None]
    partial_sum = partial_sum + self_term.reshape(copies * tile, width)
    own_scale = lax.dynamic_slice_in_dim(scale, own * tile, tile, 0)[:, None]
    halves = lax.all_to_all(partial_sum.reshape(copies, tile, width), "narrow", 0, 0, tiled=True)
    preact = jnp.sum(halves, axis=0) * own_scale
    activated = jax.nn.silu(preact).astype(jnp.bfloat16)
    sig = jax.nn.sigmoid(preact)
    own_grad = (
        cotangent.astype(jnp.float32) * sig * (1.0 + preact * (1.0 - sig)) * own_scale
    ).astype(jnp.bfloat16)
    all_grad = lax.all_gather(own_grad, "narrow", axis=0, tiled=True)
    terms = lax.dot_general(
        panel, all_grad, (((0,), (0,)), ((), ())), preferred_element_type=jnp.float32
    ).astype(jnp.bfloat16)
    weight_terms = lax.dot_general(
        aggregated, all_grad.astype(jnp.float32), (((0,), (0,)), ((), ())),
        precision=lax.Precision.HIGHEST, preferred_element_type=jnp.float32,
    ) + lax.dot_general(
        features, own_grad, (((0,), (0,)), ((), ())), preferred_element_type=jnp.float32
    )
    rows = width // owners
    high = weight_terms.astype(jnp.bfloat16)
    low = (weight_terms - high.astype(jnp.float32)).astype(jnp.bfloat16)
    payload = jnp.concatenate(
        [
            terms.reshape(owners, tile, width),
            high.reshape(owners, rows, width),
            low.reshape(owners, rows, width),
        ],
        axis=1,
    )
    received = lax.all_to_all(payload, "wide", 0, 0, tiled=True)
    band = jnp.sum(
        received[:, tile:tile + rows].astype(jnp.float32)
        + received[:, tile + rows:].astype(jnp.float32),
        axis=0,
    )
    band = lax.psum(band, "narrow").astype(jnp.bfloat16)
    grad_weight = lax.all_to_all(
        jnp.broadcast_to(band[None], (owners, rows, width)), "wide", 0, 0, tiled=True
    ).reshape(width, width).astype(jnp.float32)
    gathered_sum = jnp.sum(received[:, :tile].astype(jnp.float32), axis=0)
    message = (gathered_sum + own_grad.astype(jnp.float32)).astype(jnp.bfloat16)
    grad_features = lax.dot_general(
        message, weight, (((1,), (1,)), ((), ())), preferred_element_type=jnp.float32
    ).astype(jnp.bfloat16)
    return (activated, grad_features, grad_weight)


def solution(mesh):
    return jax.shard_map(
        per_device,
        mesh=mesh,
        in_specs=(
            P(("wide", "narrow"), None),
            P(),
            P("wide", "narrow", None),
            P("wide", "narrow"),
            P("wide", "narrow", None, None, None),
            P(("wide", "narrow"), None),
        ),
        out_specs=(P(("wide", "narrow"), None), P(("wide", "narrow"), None), P()),
        check_vma=False,
    )
```

```python
import jax
import jax.numpy as jnp
from jax import lax
from jax.sharding import PartitionSpec as P


def per_device(features, weight, tile_cols, tile_count, tile_weights, cotangent):
    tile = features.shape[0]
    width = features.shape[1]
    copies = tile_cols.shape[0]
    slots = tile_cols.shape[2]
    owners = lax.axis_size("wide")
    columns = tile_cols[:, 0, :]
    counts = tile_count[:, 0]
    tiles = tile_weights[:, 0]
    gathered_features = lax.all_gather(features, "wide", axis=0, tiled=True)
    live = (jnp.arange(slots, dtype=jnp.int32)[None, :] < counts[:, None]).astype(jnp.bfloat16)
    onehot = (columns[..., None] == jnp.arange(owners, dtype=jnp.int32)).astype(
        jnp.bfloat16
    ) * live[..., None]
    dense = jnp.einsum("skj,sktc->stjc", onehot, tiles, preferred_element_type=jnp.float32).reshape(
        copies * tile, owners * tile
    )
    degree = 1.0 + lax.psum(jnp.sum(dense, axis=1), "narrow")
    scale = lax.rsqrt(degree)
    panel = dense.astype(jnp.bfloat16)
    projected = jnp.dot(features, weight, preferred_element_type=jnp.float32).astype(jnp.bfloat16)
    own = lax.axis_index("narrow")
    aggregated = jnp.dot(panel, gathered_features, preferred_element_type=jnp.float32)
    partial_sum = jnp.dot(
        aggregated, weight.astype(jnp.float32), precision=lax.Precision.HIGHEST,
        preferred_element_type=jnp.float32,
    )
    selector = (jnp.arange(copies, dtype=jnp.int32) == own).astype(jnp.float32)
    self_term = selector[:, None, None] * projected.astype(jnp.float32)[None]
    partial_sum = partial_sum + self_term.reshape(copies * tile, width)
    own_scale = lax.dynamic_slice_in_dim(scale, own * tile, tile, 0)[:, None]
    halves = lax.all_to_all(partial_sum.reshape(copies, tile, width), "narrow", 0, 0, tiled=True)
    preact = jnp.sum(halves, axis=0) * own_scale
    activated = jax.nn.silu(preact).astype(jnp.bfloat16)
    sig = jax.nn.sigmoid(preact)
    own_grad = (
        cotangent.astype(jnp.float32) * sig * (1.0 + preact * (1.0 - sig)) * own_scale
    ).astype(jnp.bfloat16)
    all_grad = lax.all_gather(own_grad, "narrow", axis=0, tiled=True)
    terms = lax.dot_general(
        panel, all_grad, (((0,), (0,)), ((), ())), preferred_element_type=jnp.float32
    ).astype(jnp.bfloat16)
    weight_terms = lax.dot_general(
        aggregated, all_grad.astype(jnp.float32), (((0,), (0,)), ((), ())),
        precision=lax.Precision.HIGHEST, preferred_element_type=jnp.float32,
    ) + lax.dot_general(
        features, own_grad, (((0,), (0,)), ((), ())), preferred_element_type=jnp.float32
    )
    rows = width // owners
    high = weight_terms.astype(jnp.bfloat16)
    low = (weight_terms - high.astype(jnp.float32)).astype(jnp.bfloat16)
    payload = jnp.concatenate(
        [
            terms.reshape(owners, tile, width),
            high.reshape(owners, rows, width),
            low.reshape(owners, rows, width),
        ],
        axis=1,
    )
    received = lax.all_to_all(payload, "wide", 0, 0, tiled=True)
    band = jnp.sum(
        received[:, tile:tile + rows].astype(jnp.float32)
        + received[:, tile + rows:].astype(jnp.float32),
        axis=0,
    )
    pair = lax.axis_size("narrow")
    band = (band + lax.ppermute(band, "narrow", [(i, pair - 1 - i) for i in range(pair)])).astype(
        jnp.bfloat16
    )
    grad_weight = lax.all_to_all(
        jnp.broadcast_to(band[None], (owners, rows, width)), "wide", 0, 0, tiled=True
    ).reshape(width, width).astype(jnp.float32)
    gathered_sum = jnp.sum(received[:, :tile].astype(jnp.float32), axis=0)
    message = (gathered_sum + own_grad.astype(jnp.float32)).astype(jnp.bfloat16)
    grad_features = lax.dot_general(
        message, weight, (((1,), (1,)), ((), ())), preferred_element_type=jnp.float32
    ).astype(jnp.bfloat16)
    return (activated, grad_features, grad_weight)


def solution(mesh):
    return jax.shard_map(
        per_device,
        mesh=mesh,
        in_specs=(
            P(("wide", "narrow"), None),
            P(),
            P("wide", "narrow", None),
            P("wide", "narrow"),
            P("wide", "narrow", None, None, None),
            P(("wide", "narrow"), None),
        ),
        out_specs=(P(("wide", "narrow"), None), P(("wide", "narrow"), None), P()),
        check_vma=False,
    )
```

```python
import jax
import jax.numpy as jnp
from jax import lax
from jax.sharding import PartitionSpec as P


def per_device(features, weight, tile_cols, tile_count, tile_weights, cotangent):
    tile = features.shape[0]
    width = features.shape[1]
    copies = tile_cols.shape[0]
    slots = tile_cols.shape[2]
    owners = lax.axis_size("wide")
    columns = tile_cols[:, 0, :]
    counts = tile_count[:, 0]
    tiles = tile_weights[:, 0]
    gathered_features = lax.all_gather(features, "wide", axis=0, tiled=True)
    live = (jnp.arange(slots, dtype=jnp.int32)[None, :] < counts[:, None]).astype(jnp.bfloat16)
    onehot = (columns[..., None] == jnp.arange(owners, dtype=jnp.int32)).astype(
        jnp.bfloat16
    ) * live[..., None]
    dense = jnp.einsum("skj,sktc->stjc", onehot, tiles, preferred_element_type=jnp.float32).reshape(
        copies * tile, owners * tile
    )
    degree = 1.0 + lax.psum(jnp.sum(dense, axis=1), "narrow")
    scale = lax.rsqrt(degree)
    panel = dense.astype(jnp.bfloat16)
    panel, scale = lax.optimization_barrier((panel, scale))
    projected = jnp.dot(features, weight, preferred_element_type=jnp.float32).astype(jnp.bfloat16)
    own = lax.axis_index("narrow")
    aggregated = jnp.dot(panel, gathered_features, preferred_element_type=jnp.float32)
    partial_sum = jnp.dot(
        aggregated, weight.astype(jnp.float32), precision=lax.Precision.HIGHEST,
        preferred_element_type=jnp.float32,
    )
    selector = (jnp.arange(copies, dtype=jnp.int32) == own).astype(jnp.float32)
    self_term = selector[:, None, None] * projected.astype(jnp.float32)[None]
    partial_sum = partial_sum + self_term.reshape(copies * tile, width)
    own_scale = lax.dynamic_slice_in_dim(scale, own * tile, tile, 0)[:, None]
    pair = lax.axis_size("narrow")
    mine = lax.dynamic_slice_in_dim(partial_sum, own * tile, tile, 0)
    theirs = lax.dynamic_slice_in_dim(partial_sum, (pair - 1 - own) * tile, tile, 0)
    theirs = lax.ppermute(theirs, "narrow", [(i, pair - 1 - i) for i in range(pair)])
    preact = (mine + theirs) * own_scale
    activated = jax.nn.silu(preact).astype(jnp.bfloat16)
    sig = jax.nn.sigmoid(preact)
    own_grad = (
        cotangent.astype(jnp.float32) * sig * (1.0 + preact * (1.0 - sig)) * own_scale
    ).astype(jnp.bfloat16)
    all_grad = lax.all_gather(own_grad, "narrow", axis=0, tiled=True)
    terms = lax.dot_general(
        panel, all_grad, (((0,), (0,)), ((), ())), preferred_element_type=jnp.float32
    ).astype(jnp.bfloat16)
    weight_terms = lax.dot_general(
        aggregated, all_grad.astype(jnp.float32), (((0,), (0,)), ((), ())),
        precision=lax.Precision.HIGHEST, preferred_element_type=jnp.float32,
    ) + lax.dot_general(
        features, own_grad, (((0,), (0,)), ((), ())), preferred_element_type=jnp.float32
    )
    rows = width // owners
    high = weight_terms.astype(jnp.bfloat16)
    low = (weight_terms - high.astype(jnp.float32)).astype(jnp.bfloat16)
    payload = jnp.concatenate(
        [
            terms.reshape(owners, tile, width),
            high.reshape(owners, rows, width),
            low.reshape(owners, rows, width),
        ],
        axis=1,
    )
    received = lax.all_to_all(payload, "wide", 0, 0, tiled=True)
    band = jnp.sum(
        received[:, tile:tile + rows].astype(jnp.float32)
        + received[:, tile + rows:].astype(jnp.float32),
        axis=0,
    )
    band = (band + lax.ppermute(band, "narrow", [(i, pair - 1 - i) for i in range(pair)])).astype(
        jnp.bfloat16
    )
    grad_weight = lax.all_to_all(
        jnp.broadcast_to(band[None], (owners, rows, width)), "wide", 0, 0, tiled=True
    ).reshape(width, width).astype(jnp.float32)
    gathered_sum = jnp.sum(received[:, :tile].astype(jnp.float32), axis=0)
    message = (gathered_sum + own_grad.astype(jnp.float32)).astype(jnp.bfloat16)
    grad_features = lax.dot_general(
        message, weight, (((1,), (1,)), ((), ())), preferred_element_type=jnp.float32
    ).astype(jnp.bfloat16)
    return (activated, grad_features, grad_weight)


def solution(mesh):
    return jax.shard_map(
        per_device,
        mesh=mesh,
        in_specs=(
            P(("wide", "narrow"), None),
            P(),
            P("wide", "narrow", None),
            P("wide", "narrow"),
            P("wide", "narrow", None, None, None),
            P(("wide", "narrow"), None),
        ),
        out_specs=(P(("wide", "narrow"), None), P(("wide", "narrow"), None), P()),
        check_vma=False,
    )
```

```python
import jax
import jax.numpy as jnp
from jax import lax
from jax.sharding import PartitionSpec as P


def per_device(features, weight, tile_cols, tile_count, tile_weights, cotangent):
    tile = features.shape[0]
    width = features.shape[1]
    copies = tile_cols.shape[0]
    slots = tile_cols.shape[2]
    owners = lax.axis_size("wide")
    columns = tile_cols[:, 0, :]
    counts = tile_count[:, 0]
    tiles = tile_weights[:, 0]
    gathered_features = lax.all_gather(features, "wide", axis=0, tiled=True)
    live = (jnp.arange(slots, dtype=jnp.int32)[None, :] < counts[:, None]).astype(jnp.bfloat16)
    onehot = (columns[..., None] == jnp.arange(owners, dtype=jnp.int32)).astype(
        jnp.bfloat16
    ) * live[..., None]
    dense = jnp.einsum("skj,sktc->stjc", onehot, tiles, preferred_element_type=jnp.float32).reshape(
        copies * tile, owners * tile
    )
    degree = 1.0 + lax.psum(jnp.sum(dense, axis=1), "narrow")
    scale = lax.rsqrt(degree)
    panel = dense.astype(jnp.bfloat16)
    panel, scale = lax.optimization_barrier((panel, scale))
    projected = jnp.dot(features, weight, preferred_element_type=jnp.float32).astype(jnp.bfloat16)
    own = lax.axis_index("narrow")
    aggregated = jnp.dot(panel, gathered_features, preferred_element_type=jnp.float32)
    partial_sum = jnp.dot(
        aggregated, weight.astype(jnp.float32), precision=lax.Precision.HIGHEST,
        preferred_element_type=jnp.float32,
    )
    selector = (jnp.arange(copies, dtype=jnp.int32) == own).astype(jnp.float32)
    self_term = selector[:, None, None] * projected.astype(jnp.float32)[None]
    partial_sum = partial_sum + self_term.reshape(copies * tile, width)
    pair = lax.axis_size("narrow")
    theirs = lax.ppermute(partial_sum, "narrow", [(i, pair - 1 - i) for i in range(pair)])
    preact_both = (partial_sum + theirs) * scale[:, None]
    sig = jax.nn.sigmoid(preact_both)
    cot_both = lax.all_gather(cotangent, "narrow", axis=0, tiled=True).astype(jnp.float32)
    all_grad = (
        cot_both * sig * (1.0 + preact_both * (1.0 - sig)) * scale[:, None]
    ).astype(jnp.bfloat16)
    preact = lax.dynamic_slice_in_dim(preact_both, own * tile, tile, 0)
    activated = jax.nn.silu(preact).astype(jnp.bfloat16)
    own_grad = lax.dynamic_slice_in_dim(all_grad, own * tile, tile, 0)
    terms = lax.dot_general(
        panel, all_grad, (((0,), (0,)), ((), ())), preferred_element_type=jnp.float32
    ).astype(jnp.bfloat16)
    weight_terms = lax.dot_general(
        aggregated, all_grad.astype(jnp.float32), (((0,), (0,)), ((), ())),
        precision=lax.Precision.HIGHEST, preferred_element_type=jnp.float32,
    ) + lax.dot_general(
        features, own_grad, (((0,), (0,)), ((), ())), preferred_element_type=jnp.float32
    )
    rows = width // owners
    high = weight_terms.astype(jnp.bfloat16)
    low = (weight_terms - high.astype(jnp.float32)).astype(jnp.bfloat16)
    payload = jnp.concatenate(
        [
            terms.reshape(owners, tile, width),
            high.reshape(owners, rows, width),
            low.reshape(owners, rows, width),
        ],
        axis=1,
    )
    received = lax.all_to_all(payload, "wide", 0, 0, tiled=True)
    band = jnp.sum(
        received[:, tile:tile + rows].astype(jnp.float32)
        + received[:, tile + rows:].astype(jnp.float32),
        axis=0,
    )
    band = (band + lax.ppermute(band, "narrow", [(i, pair - 1 - i) for i in range(pair)])).astype(
        jnp.bfloat16
    )
    grad_weight = lax.all_to_all(
        jnp.broadcast_to(band[None], (owners, rows, width)), "wide", 0, 0, tiled=True
    ).reshape(width, width).astype(jnp.float32)
    gathered_sum = jnp.sum(received[:, :tile].astype(jnp.float32), axis=0)
    message = (gathered_sum + own_grad.astype(jnp.float32)).astype(jnp.bfloat16)
    grad_features = lax.dot_general(
        message, weight, (((1,), (1,)), ((), ())), preferred_element_type=jnp.float32
    ).astype(jnp.bfloat16)
    return (activated, grad_features, grad_weight)


def solution(mesh):
    return jax.shard_map(
        per_device,
        mesh=mesh,
        in_specs=(
            P(("wide", "narrow"), None),
            P(),
            P("wide", "narrow", None),
            P("wide", "narrow"),
            P("wide", "narrow", None, None, None),
            P(("wide", "narrow"), None),
        ),
        out_specs=(P(("wide", "narrow"), None), P(("wide", "narrow"), None), P()),
        check_vma=False,
    )
```

```python
import jax
import jax.numpy as jnp
from jax import lax
from jax.sharding import PartitionSpec as P


def per_device(features, weight, tile_cols, tile_count, tile_weights, cotangent):
    tile = features.shape[0]
    width = features.shape[1]
    copies = tile_cols.shape[0]
    slots = tile_cols.shape[2]
    owners = lax.axis_size("wide")
    columns = tile_cols[:, 0, :]
    counts = tile_count[:, 0]
    tiles = tile_weights[:, 0]
    gathered_features = lax.all_gather(features, "wide", axis=0, tiled=True)
    live = (jnp.arange(slots, dtype=jnp.int32)[None, :] < counts[:, None]).astype(jnp.bfloat16)
    onehot = (columns[..., None] == jnp.arange(owners, dtype=jnp.int32)).astype(
        jnp.bfloat16
    ) * live[..., None]
    dense = jnp.einsum("skj,sktc->stjc", onehot, tiles, preferred_element_type=jnp.float32).reshape(
        copies * tile, owners * tile
    )
    degree = 1.0 + lax.psum(jnp.sum(dense, axis=1), "narrow")
    scale = lax.rsqrt(degree)
    panel = dense.astype(jnp.bfloat16)
    panel_t = jnp.einsum(
        "skj,sktc->jcst", onehot, tiles, preferred_element_type=jnp.float32
    ).reshape(owners * tile, copies * tile).astype(jnp.bfloat16)
    panel, panel_t, scale = lax.optimization_barrier((panel, panel_t, scale))
    projected = jnp.dot(features, weight, preferred_element_type=jnp.float32).astype(jnp.bfloat16)
    own = lax.axis_index("narrow")
    aggregated = jnp.dot(panel, gathered_features, preferred_element_type=jnp.float32)
    partial_sum = jnp.dot(
        aggregated, weight.astype(jnp.float32), precision=lax.Precision.HIGHEST,
        preferred_element_type=jnp.float32,
    )
    selector = (jnp.arange(copies, dtype=jnp.int32) == own).astype(jnp.float32)
    self_term = selector[:, None, None] * projected.astype(jnp.float32)[None]
    partial_sum = partial_sum + self_term.reshape(copies * tile, width)
    pair = lax.axis_size("narrow")
    theirs = lax.ppermute(partial_sum, "narrow", [(i, pair - 1 - i) for i in range(pair)])
    preact_both = (partial_sum + theirs) * scale[:, None]
    sig = jax.nn.sigmoid(preact_both)
    cot_both = lax.all_gather(cotangent, "narrow", axis=0, tiled=True).astype(jnp.float32)
    all_grad = (
        cot_both * sig * (1.0 + preact_both * (1.0 - sig)) * scale[:, None]
    ).astype(jnp.bfloat16)
    preact = lax.dynamic_slice_in_dim(preact_both, own * tile, tile, 0)
    activated = jax.nn.silu(preact).astype(jnp.bfloat16)
    own_grad = lax.dynamic_slice_in_dim(all_grad, own * tile, tile, 0)
    terms = jnp.dot(panel_t, all_grad, preferred_element_type=jnp.float32).astype(jnp.bfloat16)
    weight_terms = lax.dot_general(
        aggregated, all_grad.astype(jnp.float32), (((0,), (0,)), ((), ())),
        precision=lax.Precision.HIGHEST, preferred_element_type=jnp.float32,
    ) + lax.dot_general(
        features, own_grad, (((0,), (0,)), ((), ())), preferred_element_type=jnp.float32
    )
    rows = width // owners
    high = weight_terms.astype(jnp.bfloat16)
    low = (weight_terms - high.astype(jnp.float32)).astype(jnp.bfloat16)
    payload = jnp.concatenate(
        [
            terms.reshape(owners, tile, width),
            high.reshape(owners, rows, width),
            low.reshape(owners, rows, width),
        ],
        axis=1,
    )
    received = lax.all_to_all(payload, "wide", 0, 0, tiled=True)
    band = jnp.sum(
        received[:, tile:tile + rows].astype(jnp.float32)
        + received[:, tile + rows:].astype(jnp.float32),
        axis=0,
    )
    band = (band + lax.ppermute(band, "narrow", [(i, pair - 1 - i) for i in range(pair)])).astype(
        jnp.bfloat16
    )
    grad_weight = lax.all_to_all(
        jnp.broadcast_to(band[None], (owners, rows, width)), "wide", 0, 0, tiled=True
    ).reshape(width, width).astype(jnp.float32)
    gathered_sum = jnp.sum(received[:, :tile].astype(jnp.float32), axis=0)
    message = (gathered_sum + own_grad.astype(jnp.float32)).astype(jnp.bfloat16)
    grad_features = lax.dot_general(
        message, weight, (((1,), (1,)), ((), ())), preferred_element_type=jnp.float32
    ).astype(jnp.bfloat16)
    return (activated, grad_features, grad_weight)


def solution(mesh):
    return jax.shard_map(
        per_device,
        mesh=mesh,
        in_specs=(
            P(("wide", "narrow"), None),
            P(),
            P("wide", "narrow", None),
            P("wide", "narrow"),
            P("wide", "narrow", None, None, None),
            P(("wide", "narrow"), None),
        ),
        out_specs=(P(("wide", "narrow"), None), P(("wide", "narrow"), None), P()),
        check_vma=False,
    )
```

```python
import jax
import jax.numpy as jnp
from jax import lax
from jax.sharding import PartitionSpec as P


def per_device(features, weight, tile_cols, tile_count, tile_weights, cotangent):
    tile = features.shape[0]
    width = features.shape[1]
    copies = tile_cols.shape[0]
    slots = tile_cols.shape[2]
    owners = lax.axis_size("wide")
    columns = tile_cols[:, 0, :]
    counts = tile_count[:, 0]
    tiles = tile_weights[:, 0]
    gathered_features = lax.all_gather(features, "wide", axis=0, tiled=True)
    live = (jnp.arange(slots, dtype=jnp.int32)[None, :] < counts[:, None]).astype(jnp.bfloat16)
    onehot = (columns[..., None] == jnp.arange(owners, dtype=jnp.int32)).astype(
        jnp.bfloat16
    ) * live[..., None]
    dense = jnp.einsum("skj,sktc->stjc", onehot, tiles, preferred_element_type=jnp.float32).reshape(
        copies * tile, owners * tile
    )
    degree = 1.0 + lax.psum(jnp.sum(dense, axis=1), "narrow")
    scale = lax.rsqrt(degree)
    panel = dense.astype(jnp.bfloat16)
    panel_t = jnp.einsum(
        "skj,sktc->jcst", onehot, tiles, preferred_element_type=jnp.float32
    ).reshape(owners * tile, copies * tile).astype(jnp.bfloat16)
    cot_both = lax.all_gather(cotangent, "narrow", axis=0, tiled=True)
    panel, panel_t, scale, cot_both = lax.optimization_barrier((panel, panel_t, scale, cot_both))
    projected = jnp.dot(features, weight, preferred_element_type=jnp.float32).astype(jnp.bfloat16)
    own = lax.axis_index("narrow")
    aggregated = jnp.dot(panel, gathered_features, preferred_element_type=jnp.float32)
    partial_sum = jnp.dot(
        aggregated, weight.astype(jnp.float32), precision=lax.Precision.HIGHEST,
        preferred_element_type=jnp.float32,
    )
    selector = (jnp.arange(copies, dtype=jnp.int32) == own).astype(jnp.float32)
    self_term = selector[:, None, None] * projected.astype(jnp.float32)[None]
    partial_sum = partial_sum + self_term.reshape(copies * tile, width)
    pair = lax.axis_size("narrow")
    theirs = lax.ppermute(partial_sum, "narrow", [(i, pair - 1 - i) for i in range(pair)])
    preact_both = (partial_sum + theirs) * scale[:, None]
    sig = jax.nn.sigmoid(preact_both)
    cot_both = cot_both.astype(jnp.float32)
    all_grad = (
        cot_both * sig * (1.0 + preact_both * (1.0 - sig)) * scale[:, None]
    ).astype(jnp.bfloat16)
    preact = lax.dynamic_slice_in_dim(preact_both, own * tile, tile, 0)
    activated = jax.nn.silu(preact).astype(jnp.bfloat16)
    own_grad = lax.dynamic_slice_in_dim(all_grad, own * tile, tile, 0)
    terms = jnp.dot(panel_t, all_grad, preferred_element_type=jnp.float32).astype(jnp.bfloat16)
    weight_terms = lax.dot_general(
        aggregated, all_grad.astype(jnp.float32), (((0,), (0,)), ((), ())),
        precision=lax.Precision.HIGHEST, preferred_element_type=jnp.float32,
    ) + lax.dot_general(
        features, own_grad, (((0,), (0,)), ((), ())), preferred_element_type=jnp.float32
    )
    rows = width // owners
    high = weight_terms.astype(jnp.bfloat16)
    low = (weight_terms - high.astype(jnp.float32)).astype(jnp.bfloat16)
    payload = jnp.concatenate(
        [
            terms.reshape(owners, tile, width),
            high.reshape(owners, rows, width),
            low.reshape(owners, rows, width),
        ],
        axis=1,
    )
    received = lax.all_to_all(payload, "wide", 0, 0, tiled=True)
    band = jnp.sum(
        received[:, tile:tile + rows].astype(jnp.float32)
        + received[:, tile + rows:].astype(jnp.float32),
        axis=0,
    )
    band = (band + lax.ppermute(band, "narrow", [(i, pair - 1 - i) for i in range(pair)])).astype(
        jnp.bfloat16
    )
    grad_weight = lax.all_to_all(
        jnp.broadcast_to(band[None], (owners, rows, width)), "wide", 0, 0, tiled=True
    ).reshape(width, width).astype(jnp.float32)
    gathered_sum = jnp.sum(received[:, :tile].astype(jnp.float32), axis=0)
    message = (gathered_sum + own_grad.astype(jnp.float32)).astype(jnp.bfloat16)
    grad_features = lax.dot_general(
        message, weight, (((1,), (1,)), ((), ())), preferred_element_type=jnp.float32
    ).astype(jnp.bfloat16)
    return (activated, grad_features, grad_weight)


def solution(mesh):
    return jax.shard_map(
        per_device,
        mesh=mesh,
        in_specs=(
            P(("wide", "narrow"), None),
            P(),
            P("wide", "narrow", None),
            P("wide", "narrow"),
            P("wide", "narrow", None, None, None),
            P(("wide", "narrow"), None),
        ),
        out_specs=(P(("wide", "narrow"), None), P(("wide", "narrow"), None), P()),
        check_vma=False,
    )
```
